512 devices in a mesh: ao: 64 (over y, z), aux: 8 (over x, core).
Axes of the slice: x: 4, y: 8, z: 8, core: 2. Of those that a mesh axis runs over, the one named last changes fastest.
Arguments:
- pair_rows: bfloat16 [8, 8192, 6000], P('aux', 'ao'), may hold values from -6 to 6
- pair_list: int32 [8, 2, 8192], P('aux', None, 'ao'), may hold values from -1 to 3999, as said below
- shell_size: int32 [2000], replicated, may hold values from 1 to 5, as said below
- occ_coeff: bfloat16 [6000, 400], P('aux'), may hold values from -0.078125 to 0.078125
- vir_coeff: bfloat16 [6000, 5504], P(None, 'ao'), may hold values from -0.078125 to 0.078125
Outputs:
- mo_ints: bfloat16 [16, 400, 5504], P(None, 'aux', 'ao')
The draws below stay inside these ranges and needn't reach their ends.
Inputs may be any that keep to these rules, and one draw needn't show every extreme that they name: `shell_size`: shells come in consecutive pairs (2k, 2k + 1) whose sizes add to 6; each size is 1, 3 or 5. `pair_list`: row 1 of a live slot is less than its shell's size; empty slots hold -1 in both rows. Within one aux index no (auxiliary function, AO function) pair is named twice. Let the owner of shell s be floor(first(s) * 64 / 6000) and a producer be a block of 128 slots along ao: a producer's live slots come first, in ascending owner; no producer has more than 2 live slots for one owner, and for every aux index some owner receives exactly 2 from every producer.
All inputs are finite; a program needn't handle non-finite values.
Results may differ from the reference program's by a relative error of at most 0.005.
Values may be sent and summed in bfloat16 or wider, within the bound.
No kernel may reach another device: no remote copies, remote signals or barrier semaphores. Data moves between devices by JAX's collectives and lax.ppermute only.
A program may use at most 64 MiB of HBM per device.

```python
import jax
import jax.numpy as jnp
from jax import lax

NBF = 6000
NOCC = 400
NVIR = 5504
AUX_DEV = 2
NSHELL = 2000
CAP = 2
ROWS_DEV = 128
NAUX = 16
N_AO = 64
N_AUX = 8


def shell_helper(key):
    pick = jax.random.randint(jax.random.fold_in(key, 11), (NSHELL // 2,), 0, 3)
    lead = 1 + 2 * pick
    sizes = jnp.stack([lead, 6 - lead], axis=1).reshape(NSHELL)
    return sizes.astype(jnp.int32)


def draw_shell_size(key, part):
    return shell_helper(key)


def draw_pair_list(key, part):
    sizes = shell_helper(key)
    offsets = jnp.cumsum(sizes) - sizes
    owner_shell = offsets * N_AO // NBF
    marks = jnp.zeros((NBF,), jnp.int32).at[offsets].set(1)
    shell_of = jnp.cumsum(marks) - 1
    component = jnp.arange(NBF, dtype=jnp.int32) - offsets[shell_of]
    owner_fn = owner_shell[shell_of]
    counts = jnp.zeros((N_AO,), jnp.int32).at[owner_fn].add(1)
    ncand = AUX_DEV * NBF

    def one_group(index):
        gkey = jax.random.fold_in(key, 1000 + index)
        levels = jax.random.randint(jax.random.fold_in(gkey, 1), (N_AO,), 1, 5)
        star = jax.random.randint(jax.random.fold_in(gkey, 2), (), 0, N_AO)
        levels = jnp.where(jnp.arange(N_AO) == star, 4, levels)
        kept = jnp.minimum(AUX_DEV * counts * levels // 4, N_AO * CAP)
        cand = jnp.arange(ncand, dtype=jnp.int32)
        cand_aux = cand // NBF
        cand_basis = cand % NBF
        cand_owner = owner_fn[cand_basis]
        perm = jax.random.permutation(jax.random.fold_in(gkey, 3), ncand).astype(jnp.int32)
        order = jnp.argsort(cand_owner * ncand + perm)
        sorted_owner = cand_owner[order]
        owner_start = AUX_DEV * (jnp.cumsum(counts) - counts)
        rank = jnp.arange(ncand, dtype=jnp.int32) - owner_start[sorted_owner]
        alive = rank < kept[sorted_owner]
        kept_start = jnp.cumsum(kept) - kept
        global_slot = kept_start[sorted_owner] + rank
        producer = global_slot % N_AO
        within = global_slot // N_AO
        position = jnp.where(alive, producer * ROWS_DEV + within, N_AO * ROWS_DEV)
        sorted_aux = cand_aux[order]
        sorted_basis = cand_basis[order]
        first_row = sorted_aux * NSHELL + shell_of[sorted_basis]
        second_row = component[sorted_basis]
        out_first = jnp.full((N_AO * ROWS_DEV,), -1, jnp.int32).at[position].set(first_row, mode='drop')
        out_second = jnp.full((N_AO * ROWS_DEV,), -1, jnp.int32).at[position].set(second_row, mode='drop')
        return jnp.stack([out_first, out_second])
    return jax.vmap(one_group)(jnp.arange(N_AUX, dtype=jnp.int32))


def shard_levels(own_key, shape, shards, smallest, high):
    loudness = 1.0
    for axis_at, blocks in shards:
        steps = jax.random.uniform(jax.random.fold_in(jax.random.fold_in(own_key, 6), axis_at), (blocks,), jnp.float32, smallest / len(shards), high / len(shards))
        loudness = loudness * jnp.repeat(jnp.exp(steps), shape[axis_at] // blocks).reshape((-1,) + (1,) * (len(shape) - 1 - axis_at))
    return loudness


def normal_values(stream_key, extent, scale, most, cuts=(), kind=jnp.bfloat16):
    values = scale * jax.random.normal(stream_key, extent, jnp.float32)
    if cuts:
        values = values * shard_levels(stream_key, extent, cuts, -0.22, 0.18)
    return jnp.clip(values, -most, most).astype(kind)


def setup_inputs(seed: int = 0) -> dict:
    keys = jax.random.split(jax.random.key(seed), 6)
    return {
        "pair_rows": normal_values(keys[0], (N_AUX, N_AO * ROWS_DEV, NBF), 1.0, 6.0, ((0, 8), (1, 64))),
        "pair_list": draw_pair_list(jax.random.fold_in(keys[5], 71), 0),
        "shell_size": draw_shell_size(jax.random.fold_in(keys[5], 71), 0),
        "occ_coeff": normal_values(keys[3], (NBF, NOCC), NBF ** -0.5, 0.078125, ((0, 8),)),
        "vir_coeff": normal_values(keys[4], (NBF, NVIR), NBF ** -0.5, 0.078125, ((1, 64),)),
    }


def reference(pair_rows, pair_list, shell_size, occ_coeff, vir_coeff):
    nshell = shell_size.shape[0]
    offsets = jnp.cumsum(shell_size) - shell_size
    groups = pair_rows.shape[0]
    slots = pair_rows.shape[1]

    def first_half(block):
        return jnp.dot(block, occ_coeff, preferred_element_type=jnp.float32).astype(jnp.bfloat16)

    half_rows = lax.map(first_half, pair_rows).reshape(groups * slots, NOCC)
    tag_shell = pair_list[:, 0, :].reshape(groups * slots)
    tag_comp = pair_list[:, 1, :].reshape(groups * slots)
    live = tag_shell >= 0
    safe = jnp.where(live, tag_shell, 0)
    aux_local = safe // nshell
    shell = safe % nshell
    basis = offsets[shell] + jnp.where(live, tag_comp, 0)
    group = jnp.arange(groups * slots, dtype=jnp.int32) // slots
    aux_index = group * AUX_DEV + aux_local
    place = jnp.where(live, aux_index * NBF + basis, NAUX * NBF).astype(jnp.int32)
    half = jnp.zeros((NAUX * NBF, NOCC), jnp.bfloat16).at[place].set(half_rows, mode="drop")
    half = half.reshape(NAUX, NBF, NOCC)

    def second_half(block):
        return jnp.dot(block.T, vir_coeff, preferred_element_type=jnp.float32).astype(jnp.bfloat16)

    return lax.map(second_half, half)
```

```python
import jax
import jax.numpy as jnp
from jax import lax
from jax.sharding import PartitionSpec as P

AUX_DEV = 2


def slot_codes(tags, shell_size, n_basis):
    nshell = shell_size.shape[0]
    offsets = jnp.cumsum(shell_size) - shell_size
    live = tags[0] >= 0
    safe = jnp.where(live, tags[0], 0)
    aux_local = safe // nshell
    shell = safe % nshell
    basis = jnp.take(offsets, shell, axis=0) + jnp.where(live, tags[1], 0)
    return jnp.where(live, aux_local * n_basis + basis, -1).astype(jnp.int32)


def shards(pair_rows, pair_list, shell_size, occ_coeff, vir_coeff):
    n_basis = vir_coeff.shape[0]
    rows = pair_rows[0]
    code = slot_codes(pair_list[0], shell_size, n_basis)
    occ_full = lax.all_gather(occ_coeff, "aux", axis=0, tiled=True)
    half_rows = jnp.dot(rows, occ_full, preferred_element_type=jnp.float32).astype(jnp.bfloat16)
    codes = lax.all_gather(code, "ao", axis=0, tiled=True)
    halves = lax.all_gather(half_rows, "ao", axis=0, tiled=True)
    live = codes >= 0
    aux_local = jnp.where(live, codes // n_basis, -1)
    mu = jnp.where(live, codes % n_basis, 0)
    picked = jnp.take(vir_coeff, mu, axis=0)
    zero = jnp.zeros((), vir_coeff.dtype)
    coeff = jnp.concatenate(
        [jnp.where((aux_local == p)[:, None], picked, zero) for p in range(AUX_DEV)], axis=1
    )
    mo = lax.dot_general(
        halves, coeff, (((0,), (0,)), ((), ())), preferred_element_type=jnp.float32
    )
    n_occ = halves.shape[1]
    n_vir = vir_coeff.shape[1]
    tiles = mo.astype(jnp.bfloat16).reshape(n_occ, AUX_DEV, n_vir).transpose(1, 0, 2)
    return lax.all_to_all(tiles, "aux", split_axis=1, concat_axis=0, tiled=True)


def solution(mesh):
    placed = (P("aux", "ao", None), P("aux", None, "ao"), P(), P("aux", None), P(None, "ao"))
    return jax.shard_map(
        shards, mesh=mesh, in_specs=placed, out_specs=P(None, "aux", "ao"), check_vma=False
    )
```

```python
import jax
import jax.numpy as jnp
import numpy as np
from jax import lax
from jax.sharding import Mesh
from jax.sharding import PartitionSpec as P

AUX_DEV = 2


def slot_codes(tags, shell_size, n_basis):
    nshell = shell_size.shape[0]
    offsets = jnp.cumsum(shell_size) - shell_size
    live = tags[0] >= 0
    safe = jnp.where(live, tags[0], 0)
    aux_local = safe // nshell
    shell = safe % nshell
    basis = jnp.take(offsets, shell, axis=0) + jnp.where(live, tags[1], 0)
    return jnp.where(live, aux_local * n_basis + basis, -1).astype(jnp.int32)


def gather_ao(x):
    x = lax.all_gather(x, "z", axis=0, tiled=True)
    return lax.all_gather(x, "y", axis=0, tiled=True)


def shards(pair_rows, pair_list, shell_size, occ_coeff, vir_coeff):
    n_basis = vir_coeff.shape[0]
    n_aux = lax.axis_size("x") * lax.axis_size("c")
    rows = pair_rows[0]
    code = slot_codes(pair_list[0], shell_size, n_basis)
    codes = gather_ao(code)
    occ_blocks = lax.all_gather(occ_coeff, ("x", "c"), axis=0)
    block_rows = rows.reshape(rows.shape[0], n_aux, occ_coeff.shape[0])
    half_rows = jnp.einsum(
        "cbn,bni->ci", block_rows, occ_blocks, preferred_element_type=jnp.float32
    ).astype(jnp.bfloat16)
    halves = gather_ao(half_rows)
    live = codes >= 0
    aux_local = jnp.where(live, codes // n_basis, -1)
    mu = jnp.where(live, codes % n_basis, 0)
    picked = jnp.take(vir_coeff, mu, axis=0)
    zero = jnp.zeros((), vir_coeff.dtype)
    coeff = jnp.concatenate(
        [jnp.where((aux_local == p)[:, None], picked, zero) for p in range(AUX_DEV)], axis=1
    )
    mo = lax.dot_general(
        halves, coeff, (((0,), (0,)), ((), ())), preferred_element_type=jnp.float32
    )
    n_occ = halves.shape[1]
    n_vir = vir_coeff.shape[1]
    tiles = mo.astype(jnp.bfloat16).reshape(n_occ, AUX_DEV, n_vir).transpose(1, 0, 2)
    return lax.all_to_all(tiles, ("x", "c"), split_axis=1, concat_axis=0, tiled=True)


def solution(mesh):
    n_ao, n_aux = mesh.devices.shape
    side = int(round(np.sqrt(n_ao)))
    fine = Mesh(mesh.devices.reshape(side, n_ao // side, n_aux // 2, 2), ("y", "z", "x", "c"))
    ao, aux = ("y", "z"), ("x", "c")
    placed = (P(aux, ao, None), P(aux, None, ao), P(), P(aux, None), P(None, ao))
    return jax.shard_map(
        shards, mesh=fine, in_specs=placed, out_specs=P(None, aux, ao), check_vma=False
    )
```

```python
import jax
import jax.numpy as jnp
import numpy as np
from jax import lax
from jax.sharding import Mesh
from jax.sharding import PartitionSpec as P

AUX_DEV = 2


def slot_codes(tags, shell_size, n_basis):
    nshell = shell_size.shape[0]
    offsets = jnp.cumsum(shell_size) - shell_size
    live = tags[0] >= 0
    safe = jnp.where(live, tags[0], 0)
    aux_local = safe // nshell
    shell = safe % nshell
    basis = jnp.take(offsets, shell, axis=0) + jnp.where(live, tags[1], 0)
    return jnp.where(live, aux_local * n_basis + basis, -1).astype(jnp.int32)


def gather_codes(code, ao, rows=64, base=128):
    code1 = code + 1
    parts = jnp.stack([code1 // base, code1 % base]).astype(jnp.bfloat16)
    block = jnp.concatenate([parts, jnp.zeros((rows - 2, code.shape[0]), jnp.bfloat16)])
    got = lax.all_gather(block, ao, axis=0).astype(jnp.int32)
    return (got[:, 0, :] * base + got[:, 1, :] - 1).reshape(-1)


def shards(pair_rows, pair_list, shell_size, occ_coeff, vir_coeff):
    n_basis = vir_coeff.shape[0]
    n_aux = lax.axis_size("x") * lax.axis_size("c")
    rows = pair_rows[0]
    code = slot_codes(pair_list[0], shell_size, n_basis)
    codes = gather_codes(code, ("y", "z"))
    occ_blocks = lax.all_gather(occ_coeff, ("x", "c"), axis=0)
    block_rows = rows.reshape(rows.shape[0], n_aux, occ_coeff.shape[0])
    half_rows = jnp.einsum(
        "cbn,bni->ci", block_rows, occ_blocks, preferred_element_type=jnp.float32
    ).astype(jnp.bfloat16)
    halves = lax.all_gather(half_rows, ("y", "z"), axis=0, tiled=True)
    live = codes >= 0
    aux_local = jnp.where(live, codes // n_basis, -1)
    mu = jnp.where(live, codes % n_basis, 0)
    picked = jnp.take(vir_coeff, mu, axis=0)
    zero = jnp.zeros((), vir_coeff.dtype)
    coeff = jnp.concatenate(
        [jnp.where((aux_local == p)[:, None], picked, zero) for p in range(AUX_DEV)], axis=1
    )
    mo = lax.dot_general(
        halves, coeff, (((0,), (0,)), ((), ())), preferred_element_type=jnp.float32
    )
    n_occ = halves.shape[1]
    n_vir = vir_coeff.shape[1]
    tiles = mo.astype(jnp.bfloat16).reshape(n_occ, AUX_DEV, n_vir).transpose(1, 0, 2)
    return lax.all_to_all(tiles, ("x", "c"), split_axis=1, concat_axis=0, tiled=True)


def solution(mesh):
    n_ao, n_aux = mesh.devices.shape
    side = int(round(np.sqrt(n_ao)))
    fine = Mesh(mesh.devices.reshape(side, n_ao // side, n_aux // 2, 2), ("y", "z", "x", "c"))
    ao, aux = ("y", "z"), ("x", "c")
    placed = (P(aux, ao, None), P(aux, None, ao), P(), P(aux, None), P(None, ao))
    return jax.shard_map(
        shards, mesh=fine, in_specs=placed, out_specs=P(None, aux, ao), check_vma=False
    )
```

```python
import jax
import jax.numpy as jnp
import numpy as np
from jax import lax
from jax.sharding import Mesh
from jax.sharding import PartitionSpec as P

AUX_DEV = 2
CODE_BASE = 128


def slot_codes(tags, shell_size, n_basis):
    nshell = shell_size.shape[0]
    offsets = jnp.cumsum(shell_size) - shell_size
    live = tags[0] >= 0
    safe = jnp.where(live, tags[0], 0)
    aux_local = safe // nshell
    shell = safe % nshell
    basis = jnp.take(offsets, shell, axis=0) + jnp.where(live, tags[1], 0)
    return jnp.where(live, aux_local * n_basis + basis, -1).astype(jnp.int32)


def gather_ao(x):
    x = lax.all_gather(x, "z", axis=0, tiled=True)
    return lax.all_gather(x, "y", axis=0, tiled=True)


def half_block(rows, occ_cols):
    occ_blocks = lax.all_gather(occ_cols, ("x", "c"), axis=0)
    return jnp.einsum(
        "cbn,bni->ci", rows, occ_blocks, preferred_element_type=jnp.float32
    ).astype(jnp.bfloat16)


def shards(pair_rows, pair_list, shell_size, occ_coeff, vir_coeff):
    n_basis = vir_coeff.shape[0]
    n_occ = occ_coeff.shape[1]
    n_vir = vir_coeff.shape[1]
    n_aux = lax.axis_size("x") * lax.axis_size("c")
    rows = pair_rows[0]
    block_rows = rows.reshape(rows.shape[0], n_aux, occ_coeff.shape[0])
    code1 = slot_codes(pair_list[0], shell_size, n_basis) + 1
    code_cols = jnp.stack([code1 // CODE_BASE, code1 % CODE_BASE], axis=1).astype(jnp.bfloat16)
    split = n_occ // 2
    first = jnp.concatenate([half_block(block_rows, occ_coeff[:, :split]), code_cols], axis=1)
    first_all = gather_ao(first)
    second = half_block(block_rows, occ_coeff[:, split:])
    second_all = gather_ao(second)
    got = first_all[:, split:].astype(jnp.int32)
    codes = got[:, 0] * CODE_BASE + got[:, 1] - 1
    live = codes >= 0
    aux_local = jnp.where(live, codes // n_basis, -1)
    mu = jnp.where(live, codes % n_basis, 0)
    picked = jnp.take(vir_coeff, mu, axis=0)
    zero = jnp.zeros((), vir_coeff.dtype)
    coeff = jnp.concatenate(
        [jnp.where((aux_local == p)[:, None], picked, zero) for p in range(AUX_DEV)], axis=1
    )
    dims = (((0,), (0,)), ((), ()))
    mo_first = lax.dot_general(first_all, coeff, dims, preferred_element_type=jnp.float32)
    mo_second = lax.dot_general(second_all, coeff, dims, preferred_element_type=jnp.float32)
    mo = jnp.concatenate([mo_first[:split], mo_second], axis=0)
    tiles = mo.astype(jnp.bfloat16).reshape(n_occ, AUX_DEV, n_vir).transpose(1, 0, 2)
    return lax.all_to_all(tiles, ("x", "c"), split_axis=1, concat_axis=0, tiled=True)


def solution(mesh):
    n_ao, n_aux = mesh.devices.shape
    side = int(round(np.sqrt(n_ao)))
    fine = Mesh(mesh.devices.reshape(side, n_ao // side, n_aux // 2, 2), ("y", "z", "x", "c"))
    ao, aux = ("y", "z"), ("x", "c")
    placed = (P(aux, ao, None), P(aux, None, ao), P(), P(aux, None), P(None, ao))
    return jax.shard_map(
        shards, mesh=fine, in_specs=placed, out_specs=P(None, aux, ao), check_vma=False
    )
```

```python
import jax
import jax.numpy as jnp
from jax import lax
from jax.sharding import PartitionSpec as P

AUX_DEV = 2


def slot_codes(tags, shell_size, n_basis):
    nshell = shell_size.shape[0]
    offsets = jnp.cumsum(shell_size) - shell_size
    live = tags[0] >= 0
    safe = jnp.where(live, tags[0], 0)
    aux_local = safe // nshell
    shell = safe % nshell
    basis = jnp.take(offsets, shell, axis=0) + jnp.where(live, tags[1], 0)
    return jnp.where(live, aux_local * n_basis + basis, -1).astype(jnp.int32)


def shards(pair_rows, pair_list, shell_size, occ_coeff, vir_coeff):
    n_basis = vir_coeff.shape[0]
    rows = pair_rows[0]
    n_aux = lax.axis_size("aux")
    code = slot_codes(pair_list[0], shell_size, n_basis)
    occ_blocks = lax.all_gather(occ_coeff, "aux", axis=0)
    block_rows = rows.reshape(rows.shape[0], n_aux, occ_coeff.shape[0])
    half_rows = jnp.einsum(
        "cbn,bni->ci", block_rows, occ_blocks, preferred_element_type=jnp.float32
    ).astype(jnp.bfloat16)
    codes = lax.all_gather(code, "ao", axis=0, tiled=True)
    halves = lax.all_gather(half_rows, "ao", axis=0, tiled=True)
    live = codes >= 0
    aux_local = jnp.where(live, codes // n_basis, -1)
    mu = jnp.where(live, codes % n_basis, 0)
    picked = jnp.take(vir_coeff, mu, axis=0)
    zero = jnp.zeros((), vir_coeff.dtype)
    coeff = jnp.concatenate(
        [jnp.where((aux_local == p)[:, None], picked, zero) for p in range(AUX_DEV)], axis=1
    )
    mo = lax.dot_general(
        halves, coeff, (((0,), (0,)), ((), ())), preferred_element_type=jnp.float32
    )
    n_occ = halves.shape[1]
    n_vir = vir_coeff.shape[1]
    tiles = mo.astype(jnp.bfloat16).reshape(n_occ, AUX_DEV, n_vir).transpose(1, 0, 2)
    return lax.all_to_all(tiles, "aux", split_axis=1, concat_axis=0, tiled=True)


def solution(mesh):
    placed = (P("aux", "ao", None), P("aux", None, "ao"), P(), P("aux", None), P(None, "ao"))
    return jax.shard_map(
        shards, mesh=mesh, in_specs=placed, out_specs=P(None, "aux", "ao"), check_vma=False
    )
```

```python
import jax
import jax.numpy as jnp
from jax import lax
from jax.sharding import Mesh
from jax.sharding import PartitionSpec as P

AUX_DEV = 2


def slot_codes(tags, shell_size, n_basis):
    nshell = shell_size.shape[0]
    offsets = jnp.cumsum(shell_size) - shell_size
    live = tags[0] >= 0
    safe = jnp.where(live, tags[0], 0)
    aux_local = safe // nshell
    shell = safe % nshell
    basis = jnp.take(offsets, shell, axis=0) + jnp.where(live, tags[1], 0)
    return jnp.where(live, aux_local * n_basis + basis, -1).astype(jnp.int32)


def shards(pair_rows, pair_list, shell_size, occ_coeff, vir_coeff):
    n_basis = vir_coeff.shape[0]
    rows = pair_rows[0]
    n_aux = lax.axis_size("x") * lax.axis_size("c")
    code = slot_codes(pair_list[0], shell_size, n_basis)
    occ_blocks = lax.all_gather(occ_coeff, ("x", "c"), axis=0)
    block_rows = rows.reshape(rows.shape[0], n_aux, occ_coeff.shape[0])
    half_rows = jnp.einsum(
        "cbn,bni->ci", block_rows, occ_blocks, preferred_element_type=jnp.float32
    ).astype(jnp.bfloat16)
    codes = lax.all_gather(code, ("z", "y"), axis=0, tiled=True)
    halves = lax.all_gather(half_rows, ("z", "y"), axis=0, tiled=True)
    live = codes >= 0
    aux_local = jnp.where(live, codes // n_basis, -1)
    mu = jnp.where(live, codes % n_basis, 0)
    picked = jnp.take(vir_coeff, mu, axis=0)
    zero = jnp.zeros((), vir_coeff.dtype)
    coeff = jnp.concatenate(
        [jnp.where((aux_local == p)[:, None], picked, zero) for p in range(AUX_DEV)], axis=1
    )
    mo = lax.dot_general(
        halves, coeff, (((0,), (0,)), ((), ())), preferred_element_type=jnp.float32
    )
    n_occ = halves.shape[1]
    n_vir = vir_coeff.shape[1]
    tiles = mo.astype(jnp.bfloat16).reshape(n_occ, AUX_DEV, n_vir).transpose(1, 0, 2)
    return lax.all_to_all(tiles, ("x", "c"), split_axis=1, concat_axis=0, tiled=True)


def solution(mesh):
    n_ao, n_aux = mesh.devices.shape
    side = int(round(n_ao ** 0.5))
    fine = Mesh(mesh.devices.reshape(side, n_ao // side, n_aux // 2, 2), ("y", "z", "x", "c"))
    ao, aux = ("y", "z"), ("x", "c")
    placed = (P(aux, ao, None), P(aux, None, ao), P(), P(aux, None), P(None, ao))
    return jax.shard_map(
        shards, mesh=fine, in_specs=placed, out_specs=P(None, aux, ao), check_vma=False
    )
```

```python
import jax
import jax.numpy as jnp
from jax import lax
from jax.sharding import Mesh
from jax.sharding import PartitionSpec as P

AUX_DEV = 2
EVERY = ("y", "z", "x", "c")


def slot_codes(tags, shell_size, n_basis):
    nshell = shell_size.shape[0]
    offsets = jnp.cumsum(shell_size) - shell_size
    live = tags[0] >= 0
    safe = jnp.where(live, tags[0], 0)
    aux_local = safe // nshell
    shell = safe % nshell
    basis = jnp.take(offsets, shell, axis=0) + jnp.where(live, tags[1], 0)
    return jnp.where(live, aux_local * n_basis + basis, -1).astype(jnp.int32)


def crossed_groups():
    ny, nz, nx, nc = (lax.axis_size(a) for a in EVERY)

    def index(y, z, x, c):
        return ((y * nz + z) * nx + x) * nc + c

    along_z = [[index(y, z, x, c) for z in range(nz)] for y in range(ny) for x in range(nx) for c in range(nc)]
    along_y = [[index(y, z, x, c) for y in range(ny)] for z in range(nz) for x in range(nx) for c in range(nc)]
    first = [g for g in along_z if g[0] % nc == 0] + [g for g in along_y if g[0] % nc == 1]
    second = [g for g in along_y if g[0] % nc == 0] + [g for g in along_z if g[0] % nc == 1]
    return first, second


def gather_ao(x, groups):
    for group in groups:
        x = lax.all_gather(x, EVERY, axis_index_groups=group, axis=0, tiled=True)
    return x


def shards(pair_rows, pair_list, shell_size, occ_coeff, vir_coeff):
    n_basis = vir_coeff.shape[0]
    n_aux = lax.axis_size("x") * lax.axis_size("c")
    groups = crossed_groups()
    rows = pair_rows[0]
    code = slot_codes(pair_list[0], shell_size, n_basis)
    codes = gather_ao(code, groups)
    occ_blocks = lax.all_gather(occ_coeff, ("x", "c"), axis=0)
    codes, occ_blocks = lax.optimization_barrier((codes, occ_blocks))
    block_rows = rows.reshape(rows.shape[0], n_aux, occ_coeff.shape[0])
    half_rows = jnp.einsum(
        "cbn,bni->ci", block_rows, occ_blocks, preferred_element_type=jnp.float32
    ).astype(jnp.bfloat16)
    halves = gather_ao(half_rows, groups)
    live = codes >= 0
    aux_local = jnp.where(live, codes // n_basis, -1)
    mu = jnp.where(live, codes % n_basis, 0)
    picked = jnp.take(vir_coeff, mu, axis=0)
    zero = jnp.zeros((), vir_coeff.dtype)
    coeff = jnp.concatenate(
        [jnp.where((aux_local == p)[:, None], picked, zero) for p in range(AUX_DEV)], axis=1
    )
    mo = lax.dot_general(
        halves, coeff, (((0,), (0,)), ((), ())), preferred_element_type=jnp.float32
    )
    n_occ = halves.shape[1]
    n_vir = vir_coeff.shape[1]
    tiles = mo.astype(jnp.bfloat16).reshape(n_occ, AUX_DEV, n_vir).transpose(1, 0, 2)
    return lax.all_to_all(tiles, ("x", "c"), split_axis=1, concat_axis=0, tiled=True)


def solution(mesh):
    n_ao, n_aux = mesh.devices.shape
    side = int(round(n_ao ** 0.5))
    fine = Mesh(mesh.devices.reshape(side, n_ao // side, n_aux // 2, 2), EVERY)
    ao, aux = ("y", "z"), ("x", "c")
    placed = (P(aux, ao, None), P(aux, None, ao), P(), P(aux, None), P(None, ao))
    return jax.shard_map(
        shards, mesh=fine, in_specs=placed, out_specs=P(None, aux, ao), check_vma=False
    )
```

```python
import jax
import jax.numpy as jnp
from jax import lax
from jax.sharding import Mesh
from jax.sharding import PartitionSpec as P

AUX_DEV = 2
EVERY = ("y", "z", "x", "c")


def slot_codes(tags, shell_size, n_basis):
    nshell = shell_size.shape[0]
    offsets = jnp.cumsum(shell_size) - shell_size
    live = tags[0] >= 0
    safe = jnp.where(live, tags[0], 0)
    aux_local = safe // nshell
    shell = safe % nshell
    basis = jnp.take(offsets, shell, axis=0) + jnp.where(live, tags[1], 0)
    return jnp.where(live, aux_local * n_basis + basis, -1).astype(jnp.int32)


def crossed_groups():
    ny, nz, nx, nc = (lax.axis_size(a) for a in EVERY)

    def index(y, z, x, c):
        return ((y * nz + z) * nx + x) * nc + c

    along_z = [[index(y, z, x, c) for z in range(nz)] for y in range(ny) for x in range(nx) for c in range(nc)]
    along_y = [[index(y, z, x, c) for y in range(ny)] for z in range(nz) for x in range(nx) for c in range(nc)]
    first = [g for g in along_z if g[0] % nc == 0] + [g for g in along_y if g[0] % nc == 1]
    second = [g for g in along_y if g[0] % nc == 0] + [g for g in along_z if g[0] % nc == 1]
    return first, second


def gather_ao(x, groups):
    for group in groups:
        x = lax.all_gather(x, EVERY, axis_index_groups=group, axis=0, tiled=True)
    return x


def gather_ao_offloaded(x, groups, rows):
    first, second = groups
    n = x.shape[0]
    padded = jnp.pad(x, ((0, rows - n), (0, 0)))
    got = lax.all_gather(padded, EVERY, axis_index_groups=first, axis=0)
    got = got[:, :n].reshape((-1,) + x.shape[1:])
    return lax.all_gather(got, EVERY, axis_index_groups=second, axis=0, tiled=True)


def shards(pair_rows, pair_list, shell_size, occ_coeff, vir_coeff):
    n_basis = vir_coeff.shape[0]
    n_aux = lax.axis_size("x") * lax.axis_size("c")
    groups = crossed_groups()
    rows = pair_rows[0]
    code = slot_codes(pair_list[0], shell_size, n_basis)
    codes = gather_ao(code, groups)
    occ_blocks = lax.all_gather(occ_coeff, ("x", "c"), axis=0)
    codes, occ_blocks = lax.optimization_barrier((codes, occ_blocks))
    block_rows = rows.reshape(rows.shape[0], n_aux, occ_coeff.shape[0])
    half_rows = jnp.einsum(
        "cbn,bni->ci", block_rows, occ_blocks, preferred_element_type=jnp.float32
    ).astype(jnp.bfloat16)
    halves = gather_ao_offloaded(half_rows, groups, 168)
    live = codes >= 0
    aux_local = jnp.where(live, codes // n_basis, -1)
    mu = jnp.where(live, codes % n_basis, 0)
    picked = jnp.take(vir_coeff, mu, axis=0)
    zero = jnp.zeros((), vir_coeff.dtype)
    coeff = jnp.concatenate(
        [jnp.where((aux_local == p)[:, None], picked, zero) for p in range(AUX_DEV)], axis=1
    )
    mo = lax.dot_general(
        halves, coeff, (((0,), (0,)), ((), ())), preferred_element_type=jnp.float32
    )
    n_occ = halves.shape[1]
    n_vir = vir_coeff.shape[1]
    tiles = mo.astype(jnp.bfloat16).reshape(n_occ, AUX_DEV, n_vir).transpose(1, 0, 2)
    return lax.all_to_all(tiles, ("x", "c"), split_axis=1, concat_axis=0, tiled=True)


def solution(mesh):
    n_ao, n_aux = mesh.devices.shape
    side = int(round(n_ao ** 0.5))
    fine = Mesh(mesh.devices.reshape(side, n_ao // side, n_aux // 2, 2), EVERY)
    ao, aux = ("y", "z"), ("x", "c")
    placed = (P(aux, ao, None), P(aux, None, ao), P(), P(aux, None), P(None, ao))
    return jax.shard_map(
        shards, mesh=fine, in_specs=placed, out_specs=P(None, aux, ao), check_vma=False
    )
```

```python
import jax
import jax.numpy as jnp
from jax import lax
from jax.sharding import Mesh
from jax.sharding import PartitionSpec as P

AUX_DEV = 2
EVERY = ("y", "z", "x", "c")


def slot_codes(tags, shell_size, n_basis):
    nshell = shell_size.shape[0]
    offsets = jnp.cumsum(shell_size) - shell_size
    live = tags[0] >= 0
    safe = jnp.where(live, tags[0], 0)
    aux_local = safe // nshell
    shell = safe % nshell
    basis = jnp.take(offsets, shell, axis=0) + jnp.where(live, tags[1], 0)
    return jnp.where(live, aux_local * n_basis + basis, -1).astype(jnp.int32)


def crossed_groups():
    ny, nz, nx, nc = (lax.axis_size(a) for a in EVERY)

    def index(y, z, x, c):
        return ((y * nz + z) * nx + x) * nc + c

    along_z = [[index(y, z, x, c) for z in range(nz)] for y in range(ny) for x in range(nx) for c in range(nc)]
    along_y = [[index(y, z, x, c) for y in range(ny)] for z in range(nz) for x in range(nx) for c in range(nc)]
    first = [g for g in along_z if g[0] % nc == 0] + [g for g in along_y if g[0] % nc == 1]
    second = [g for g in along_y if g[0] % nc == 0] + [g for g in along_z if g[0] % nc == 1]
    return first, second


def gather_ao(x, groups):
    for group in groups:
        x = lax.all_gather(x, EVERY, axis_index_groups=group, axis=0, tiled=True)
    return x


def exchange_codes(code):
    ny, nz = lax.axis_size("y"), lax.axis_size("z")
    sent = jnp.broadcast_to(code[None], (ny * nz,) + code.shape)
    got = lax.all_to_all(sent, ("y", "z"), split_axis=0, concat_axis=0, tiled=True)
    swapped = got.reshape(ny, nz, -1).transpose(1, 0, 2).reshape(got.shape)
    return jnp.where(lax.axis_index("c") == 0, got, swapped).reshape(-1)


def shards(pair_rows, pair_list, shell_size, occ_coeff, vir_coeff):
    n_basis = vir_coeff.shape[0]
    n_aux = lax.axis_size("x") * lax.axis_size("c")
    groups = crossed_groups()
    rows = pair_rows[0]
    code = slot_codes(pair_list[0], shell_size, n_basis)
    codes = exchange_codes(code)
    occ_blocks = lax.all_gather(occ_coeff, ("x", "c"), axis=0)
    codes, occ_blocks = lax.optimization_barrier((codes, occ_blocks))
    block_rows = rows.reshape(rows.shape[0], n_aux, occ_coeff.shape[0])
    half_rows = jnp.einsum(
        "cbn,bni->ci", block_rows, occ_blocks, preferred_element_type=jnp.float32
    ).astype(jnp.bfloat16)
    halves = gather_ao(half_rows, groups)
    live = codes >= 0
    aux_local = jnp.where(live, codes // n_basis, -1)
    mu = jnp.where(live, codes % n_basis, 0)
    picked = jnp.take(vir_coeff, mu, axis=0)
    zero = jnp.zeros((), vir_coeff.dtype)
    coeff = jnp.concatenate(
        [jnp.where((aux_local == p)[:, None], picked, zero) for p in range(AUX_DEV)], axis=1
    )
    mo = lax.dot_general(
        halves, coeff, (((0,), (0,)), ((), ())), preferred_element_type=jnp.float32
    )
    n_occ = halves.shape[1]
    n_vir = vir_coeff.shape[1]
    tiles = mo.astype(jnp.bfloat16).reshape(n_occ, AUX_DEV, n_vir).transpose(1, 0, 2)
    return lax.all_to_all(tiles, ("x", "c"), split_axis=1, concat_axis=0, tiled=True)


def solution(mesh):
    n_ao, n_aux = mesh.devices.shape
    side = int(round(n_ao ** 0.5))
    fine = Mesh(mesh.devices.reshape(side, n_ao // side, n_aux // 2, 2), EVERY)
    ao, aux = ("y", "z"), ("x", "c")
    placed = (P(aux, ao, None), P(aux, None, ao), P(), P(aux, None), P(None, ao))
    return jax.shard_map(
        shards, mesh=fine, in_specs=placed, out_specs=P(None, aux, ao), check_vma=False
    )
```

```python
import jax
import jax.numpy as jnp
from jax import lax
from jax.sharding import Mesh
from jax.sharding import PartitionSpec as P

AUX_DEV = 2
EVERY = ("y", "z", "x", "c")


def slot_codes(tags, shell_size, n_basis):
    nshell = shell_size.shape[0]
    offsets = jnp.cumsum(shell_size) - shell_size
    live = tags[0] >= 0
    safe = jnp.where(live, tags[0], 0)
    aux_local = safe // nshell
    shell = safe % nshell
    basis = jnp.take(offsets, shell, axis=0) + jnp.where(live, tags[1], 0)
    return jnp.where(live, aux_local * n_basis + basis, -1).astype(jnp.int32)


def crossed_groups():
    ny, nz, nx, nc = (lax.axis_size(a) for a in EVERY)

    def index(y, z, x, c):
        return ((y * nz + z) * nx + x) * nc + c

    along_z = [[index(y, z, x, c) for z in range(nz)] for y in range(ny) for x in range(nx) for c in range(nc)]
    along_y = [[index(y, z, x, c) for y in range(ny)] for z in range(nz) for x in range(nx) for c in range(nc)]
    first = [g for g in along_z if g[0] % nc == 0] + [g for g in along_y if g[0] % nc == 1]
    second = [g for g in along_y if g[0] % nc == 0] + [g for g in along_z if g[0] % nc == 1]
    return first, second


def gather_ao(x, groups):
    for group in groups:
        x = lax.all_gather(x, EVERY, axis_index_groups=group, axis=0, tiled=True)
    return x


def exchange_codes(code):
    ny, nz = lax.axis_size("y"), lax.axis_size("z")
    sent = jnp.broadcast_to(code[None], (ny * nz,) + code.shape)
    got = lax.all_to_all(sent, ("y", "z"), split_axis=0, concat_axis=0, tiled=True)
    swapped = got.reshape(ny, nz, -1).transpose(1, 0, 2).reshape(got.shape)
    return jnp.where(lax.axis_index("c") == 0, got, swapped).reshape(-1)


def shards(pair_rows, pair_list, shell_size, occ_coeff, vir_coeff):
    n_basis = vir_coeff.shape[0]
    n_aux = lax.axis_size("x") * lax.axis_size("c")
    groups = crossed_groups()
    rows = pair_rows[0]
    code = slot_codes(pair_list[0], shell_size, n_basis)
    codes = exchange_codes(code)
    occ_blocks = lax.all_gather(occ_coeff, ("x", "c"), axis=0)
    codes, occ_blocks = lax.optimization_barrier((codes, occ_blocks))
    block_rows = rows.reshape(rows.shape[0], n_aux, occ_coeff.shape[0])
    half_rows = jnp.einsum(
        "cbn,bni->ci", block_rows, occ_blocks, preferred_element_type=jnp.float32
    ).astype(jnp.bfloat16)
    halves = gather_ao(half_rows, groups)
    n_vir = vir_coeff.shape[1]
    blocks = [
        jnp.concatenate(
            [vir_coeff if p == q else jnp.zeros_like(vir_coeff) for q in range(AUX_DEV)], axis=1
        )
        for p in range(AUX_DEV)
    ]
    table = jnp.concatenate(blocks + [jnp.zeros((1, AUX_DEV * n_vir), vir_coeff.dtype)], axis=0)
    coeff = jnp.take(table, jnp.where(codes >= 0, codes, AUX_DEV * n_basis), axis=0)
    mo = lax.dot_general(
        halves, coeff, (((0,), (0,)), ((), ())), preferred_element_type=jnp.float32
    )
    n_occ = halves.shape[1]
    tiles = mo.astype(jnp.bfloat16).reshape(n_occ, AUX_DEV, n_vir).transpose(1, 0, 2)
    return lax.all_to_all(tiles, ("x", "c"), split_axis=1, concat_axis=0, tiled=True)


def solution(mesh):
    n_ao, n_aux = mesh.devices.shape
    side = int(round(n_ao ** 0.5))
    fine = Mesh(mesh.devices.reshape(side, n_ao // side, n_aux // 2, 2), EVERY)
    ao, aux = ("y", "z"), ("x", "c")
    placed = (P(aux, ao, None), P(aux, None, ao), P(), P(aux, None), P(None, ao))
    return jax.shard_map(
        shards, mesh=fine, in_specs=placed, out_specs=P(None, aux, ao), check_vma=False
    )
```

```python
import jax
import jax.numpy as jnp
from jax import lax
from jax.sharding import Mesh
from jax.sharding import PartitionSpec as P

AUX_DEV = 2
EVERY = ("y", "z", "x", "c")


def slot_codes(tags, shell_size, n_basis):
    nshell = shell_size.shape[0]
    offsets = jnp.cumsum(shell_size) - shell_size
    live = tags[0] >= 0
    safe = jnp.where(live, tags[0], 0)
    aux_local = safe // nshell
    shell = safe % nshell
    basis = jnp.take(offsets, shell, axis=0) + jnp.where(live, tags[1], 0)
    return jnp.where(live, aux_local * n_basis + basis, -1).astype(jnp.int32)


def crossed_groups():
    ny, nz, nx, nc = (lax.axis_size(a) for a in EVERY)

    def index(y, z, x, c):
        return ((y * nz + z) * nx + x) * nc + c

    along_z = [[index(y, z, x, c) for z in range(nz)] for y in range(ny) for x in range(nx) for c in range(nc)]
    along_y = [[index(y, z, x, c) for y in range(ny)] for z in range(nz) for x in range(nx) for c in range(nc)]
    first = [g for g in along_y if g[0] % nc == 0] + [g for g in along_z if g[0] % nc == 1]
    second = [g for g in along_z if g[0] % nc == 0] + [g for g in along_y if g[0] % nc == 1]
    return first, second


def gather_ao(x, groups):
    for group in groups:
        x = lax.all_gather(x, EVERY, axis_index_groups=group, axis=0, tiled=True)
    return x


def exchange_codes(code):
    ny, nz = lax.axis_size("y"), lax.axis_size("z")
    sent = jnp.broadcast_to(code[None], (ny * nz,) + code.shape)
    got = lax.all_to_all(sent, ("y", "z"), split_axis=0, concat_axis=0, tiled=True)
    swapped = got.reshape(ny, nz, -1).transpose(1, 0, 2).reshape(got.shape)
    return jnp.where(lax.axis_index("c") == 1, got, swapped).reshape(-1)


def shards(pair_rows, pair_list, shell_size, occ_coeff, vir_coeff):
    n_basis = vir_coeff.shape[0]
    n_aux = lax.axis_size("x") * lax.axis_size("c")
    groups = crossed_groups()
    rows = pair_rows[0]
    code = slot_codes(pair_list[0], shell_size, n_basis)
    codes = exchange_codes(code)
    occ_blocks = lax.all_gather(occ_coeff, ("x", "c"), axis=0)
    codes, occ_blocks = lax.optimization_barrier((codes, occ_blocks))
    block_rows = rows.reshape(rows.shape[0], n_aux, occ_coeff.shape[0])
    half_rows = jnp.einsum(
        "cbn,bni->ci", block_rows, occ_blocks, preferred_element_type=jnp.float32
    ).astype(jnp.bfloat16)
    halves = gather_ao(half_rows, groups)
    live = codes >= 0
    aux_local = jnp.where(live, codes // n_basis, -1)
    mu = jnp.where(live, codes % n_basis, 0)
    picked = jnp.take(vir_coeff, mu, axis=0)
    zero = jnp.zeros((), vir_coeff.dtype)
    coeff = jnp.concatenate(
        [jnp.where((aux_local == p)[:, None], picked, zero) for p in range(AUX_DEV)], axis=1
    )
    mo = lax.dot_general(
        halves, coeff, (((0,), (0,)), ((), ())), preferred_element_type=jnp.float32
    )
    n_occ = halves.shape[1]
    n_vir = vir_coeff.shape[1]
    tiles = mo.astype(jnp.bfloat16).reshape(n_occ, AUX_DEV, n_vir).transpose(1, 0, 2)
    return lax.all_to_all(tiles, ("x", "c"), split_axis=1, concat_axis=0, tiled=True)


def solution(mesh):
    n_ao, n_aux = mesh.devices.shape
    side = int(round(n_ao ** 0.5))
    fine = Mesh(mesh.devices.reshape(side, n_ao // side, n_aux // 2, 2), EVERY)
    ao, aux = ("y", "z"), ("x", "c")
    placed = (P(aux, ao, None), P(aux, None, ao), P(), P(aux, None), P(None, ao))
    return jax.shard_map(
        shards, mesh=fine, in_specs=placed, out_specs=P(None, aux, ao), check_vma=False
    )
```

```python
import jax
import jax.numpy as jnp
from jax import lax
from jax.sharding import Mesh
from jax.sharding import PartitionSpec as P

AUX_DEV = 2
EVERY = ("y", "z", "x", "c")


def slot_codes(tags, shell_size, n_basis):
    nshell = shell_size.shape[0]
    offsets = jnp.cumsum(shell_size) - shell_size
    live = tags[0] >= 0
    safe = jnp.where(live, tags[0], 0)
    aux_local = safe // nshell
    shell = safe % nshell
    basis = jnp.take(offsets, shell, axis=0) + jnp.where(live, tags[1], 0)
    return jnp.where(live, aux_local * n_basis + basis, -1).astype(jnp.int32)


def crossed_groups():
    ny, nz, nx, nc = (lax.axis_size(a) for a in EVERY)

    def index(y, z, x, c):
        return ((y * nz + z) * nx + x) * nc + c

    along_z = [[index(y, z, x, c) for z in range(nz)] for y in range(ny) for x in range(nx) for c in range(nc)]
    along_y = [[index(y, z, x, c) for y in range(ny)] for z in range(nz) for x in range(nx) for c in range(nc)]
    first = [g for g in along_z if g[0] % nc == 0] + [g for g in along_y if g[0] % nc == 1]
    second = [g for g in along_y if g[0] % nc == 0] + [g for g in along_z if g[0] % nc == 1]
    return first, second


def gather_ao(x, groups):
    for group in groups:
        x = lax.all_gather(x, EVERY, axis_index_groups=group, axis=0, tiled=True)
    return x


def exchange_codes(code):
    ny, nz = lax.axis_size("y"), lax.axis_size("z")
    sent = jnp.broadcast_to(code[None], (ny * nz,) + code.shape)
    got = lax.all_to_all(sent, ("y", "z"), split_axis=0, concat_axis=0, tiled=True)
    swapped = got.reshape(ny, nz, -1).transpose(1, 0, 2).reshape(got.shape)
    return jnp.where(lax.axis_index("c") == 0, got, swapped).reshape(-1)


def shards(pair_rows, pair_list, shell_size, occ_coeff, vir_coeff):
    n_basis = vir_coeff.shape[0]
    n_aux = lax.axis_size("x") * lax.axis_size("c")
    groups = crossed_groups()
    rows = pair_rows[0]
    code = slot_codes(pair_list[0], shell_size, n_basis)
    codes = exchange_codes(code)
    occ_blocks = lax.all_gather(occ_coeff, ("x", "c"), axis=0)
    codes, occ_blocks = lax.optimization_barrier((codes, occ_blocks))
    block_rows = rows.reshape(rows.shape[0], n_aux, occ_coeff.shape[0])
    half_rows = jnp.einsum(
        "cbn,bni->ci", block_rows, occ_blocks, preferred_element_type=jnp.float32
    ).astype(jnp.bfloat16)
    halves = gather_ao(half_rows, groups)
    live = codes >= 0
    aux_local = jnp.where(live, codes // n_basis, -1)
    mu = jnp.where(live, codes % n_basis, 0)
    picked = jnp.take(vir_coeff, mu, axis=0)
    zero = jnp.zeros((), vir_coeff.dtype)
    coeff = jnp.concatenate(
        [jnp.where((aux_local == p)[:, None], picked, zero) for p in range(AUX_DEV)], axis=1
    )
    mo = lax.dot_general(
        coeff, halves, (((0,), (0,)), ((), ())), preferred_element_type=jnp.float32
    )
    n_occ = halves.shape[1]
    n_vir = vir_coeff.shape[1]
    tiles = mo.astype(jnp.bfloat16).reshape(AUX_DEV, n_vir, n_occ).transpose(0, 2, 1)
    return lax.all_to_all(tiles, ("x", "c"), split_axis=1, concat_axis=0, tiled=True)


def solution(mesh):
    n_ao, n_aux = mesh.devices.shape
    side = int(round(n_ao ** 0.5))
    fine = Mesh(mesh.devices.reshape(side, n_ao // side, n_aux // 2, 2), EVERY)
    ao, aux = ("y", "z"), ("x", "c")
    placed = (P(aux, ao, None), P(aux, None, ao), P(), P(aux, None), P(None, ao))
    return jax.shard_map(
        shards, mesh=fine, in_specs=placed, out_specs=P(None, aux, ao), check_vma=False
    )
```
